32 devices in a mesh: row: 4 (over y, core), col: 8 (over z, x).
Axes of the slice: x: 2, y: 2, z: 4, core: 2. Of those that a mesh axis runs over, the one named last changes fastest.
Arguments:
- incoming: bfloat16 [8, 32, 16, 1024], P('row', 'col'), may hold values from -6 to 6
- cell_type: int32 [8, 32], P('row', 'col'), may hold values from 0 to 1
- bank: bfloat16 [4, 8, 1024, 1024], P('row', 'col'), may hold values from -0.1875 to 0.1875
- owner: int32 [2], replicated, may hold values from 0 to 31
- port_cell: int32 [16], replicated, may hold values from 0 to 255
- excite: float32 [16, 1024], replicated, may hold values from -6 to 6
Outputs:
- outgoing: bfloat16 [8, 32, 16, 1024], P('row', 'col')
The draws below stay inside these ranges and needn't reach their ends.
All inputs are finite; a program needn't handle non-finite values.
Results may differ from the reference program's by a relative error of at most 0.0057.
Values may be sent and summed in bfloat16 or wider, within the bound.
No kernel may reach another device: no remote copies, remote signals or barrier semaphores. Data moves between devices by JAX's collectives and lax.ppermute only.
A program may use at most 64 MiB of HBM per device.

```python
import jax
import jax.numpy as jnp
from jax import lax

ORD = 1024
PORTS = 16
TYPES = 2
SWEEPS = 3
NR = 8
NC = 32
N_ROW = 4
N_COL = 8


def touch_ends(values, own_key, smallest, high):
    place = [jax.random.randint(jax.random.fold_in(own_key, axis), (), 0, length) for axis, length in enumerate(values.shape)]
    main_axis = values.shape.index(max(values.shape))
    beside = place[:main_axis] + [(place[main_axis] + 1) % values.shape[main_axis]] + place[main_axis + 1:]
    return values.at[tuple(place)].set(smallest).at[tuple(beside)].set(high)


def steps_of(stream_key, shape, split, low, top_value):
    gain, own = 1.0, jax.random.fold_in(stream_key, 6)
    for dim, shards_of in split:
        draws = jnp.exp(jax.random.uniform(jax.random.fold_in(own, dim), (shards_of,), jnp.float32, low / len(split), top_value / len(split)))
        gain = gain * jnp.repeat(draws, shape[dim] // shards_of).reshape([-1 if axis == dim else 1 for axis in range(len(shape))])
    return gain


def scatter_about(rng, shape, deviation, reach, split=(), held_as=jnp.bfloat16):
    values = jax.random.normal(rng, shape, jnp.float32) * deviation
    if len(split) > 0:
        values = steps_of(rng, shape, split, -0.22, 0.18) * values
    return jnp.clip(values, min=-reach, max=reach).astype(held_as)


def setup_inputs(seed: int = 0) -> dict:
    seeds = jax.random.split(jax.random.key(seed), 7)
    return {
        "incoming": scatter_about(seeds[0], (NR, NC, PORTS, ORD), 1.0, 6.0, ((0, 4), (1, 8))),
        "cell_type": touch_ends(jax.random.randint(seeds[1], (NR, NC), 0, TYPES), jax.random.fold_in(seeds[1], 1), 0, TYPES - 1).astype(jnp.int32),
        "bank": scatter_about(seeds[2], (N_ROW, N_COL, ORD, ORD), ORD ** -0.5, 0.1875, ((0, 4), (1, 8))),
        "owner": jax.random.randint(seeds[3], (TYPES,), 0, N_ROW * N_COL).astype(jnp.int32),
        "port_cell": touch_ends(jax.random.randint(seeds[4], (PORTS,), 0, NR * NC), jax.random.fold_in(seeds[4], 1), 0, (NR * NC) - 1).astype(jnp.int32),
        "excite": scatter_about(seeds[5], (PORTS, ORD), 1.0, 6.0, (), jnp.float32),
    }


def pass_traces(outgoing):
    face_len = outgoing.shape[-1] // 4
    west_face = outgoing[..., :face_len]
    east_face = outgoing[..., face_len:2 * face_len]
    north_face = outgoing[..., 2 * face_len:3 * face_len]
    south_face = outgoing[..., 3 * face_len:]
    zero_col = jnp.zeros_like(east_face[:, :1])
    new_west = jnp.concatenate([zero_col, east_face[:, :-1]], axis=1)
    new_east = jnp.concatenate([west_face[:, 1:], zero_col], axis=1)
    zero_row = jnp.zeros_like(south_face[:1])
    new_north = jnp.concatenate([zero_row, south_face[:-1]], axis=0)
    new_south = jnp.concatenate([north_face[1:], zero_row], axis=0)
    return jnp.concatenate([new_west, new_east, new_north, new_south], axis=-1)


def reference(incoming, cell_type, bank, owner, port_cell, excite):
    operators = bank[owner // N_COL, owner % N_COL].astype(jnp.float32)
    num_rows, num_cols = cell_type.shape
    cell_count = num_rows * num_cols
    kinds = cell_type.reshape(cell_count)
    cell_ids = jnp.arange(cell_count, dtype=jnp.int32)
    traces = incoming
    outgoing = incoming
    for sweep_id in range(SWEEPS):
        flat_traces = traces.reshape(cell_count, PORTS, ORD)

        def per_cell(item):
            trace_rows, kind_id, cell_id = item
            product = jnp.dot(trace_rows.astype(jnp.float32), operators[kind_id], precision=lax.Precision.HIGHEST)
            port_hits = (port_cell == cell_id).astype(jnp.float32)
            return (product + port_hits[:, None] * excite).astype(jnp.bfloat16)

        outgoing = lax.map(per_cell, (flat_traces, kinds, cell_ids)).reshape(num_rows, num_cols, PORTS, ORD)
        if sweep_id + 1 < SWEEPS:
            traces = pass_traces(outgoing)
    return outgoing
```

```python
import jax
import jax.numpy as jnp
from jax import lax
from jax.sharding import PartitionSpec as P

TYPES = 2
SWEEPS = 3


def with_halo(block, sides, width):
    for axis, dim in sides:
        count = lax.axis_size(axis)
        forward = [(i, i + 1) for i in range(count - 1)]
        backward = [(target, source) for source, target in forward]
        low = lax.ppermute(
            lax.slice_in_dim(block, block.shape[dim] - width, None, axis=dim), axis, forward
        )
        high = lax.ppermute(lax.slice_in_dim(block, 0, width, axis=dim), axis, backward)
        block = jnp.concatenate([low, block, high], axis=dim)
    return block


def pass_traces(outgoing):
    face_len = outgoing.shape[-1] // 4
    west_face = outgoing[..., :face_len]
    east_face = outgoing[..., face_len : 2 * face_len]
    north_face = outgoing[..., 2 * face_len : 3 * face_len]
    south_face = outgoing[..., 3 * face_len :]
    side_send = jnp.stack([west_face[:, 0], east_face[:, -1]], axis=1)
    side_got = with_halo(side_send, (("col", 1),), 1)
    new_west = jnp.concatenate([side_got[:, 0][:, None], east_face[:, :-1]], axis=1)
    new_east = jnp.concatenate([west_face[:, 1:], side_got[:, 3][:, None]], axis=1)
    end_send = jnp.stack([north_face[0], south_face[-1]], axis=0)
    end_got = with_halo(end_send, (("row", 0),), 1)
    new_north = jnp.concatenate([end_got[0][None], south_face[:-1]], axis=0)
    new_south = jnp.concatenate([north_face[1:], end_got[3][None]], axis=0)
    return jnp.concatenate([new_west, new_east, new_north, new_south], axis=-1)


def masked_stack(own_operator, owner):
    me = lax.axis_index("row") * lax.axis_size("col") + lax.axis_index("col")
    return jnp.stack(
        [jnp.where(me == owner[k], own_operator, jnp.zeros_like(own_operator)) for k in range(TYPES)],
        axis=0,
    )


def broadcast(own_operator, owner):
    return lax.psum(masked_stack(own_operator, owner), ("row", "col"))


def local(incoming, cell_type, bank, owner, port_cell, excite):
    cell_rows, cell_cols, port_count, order = incoming.shape
    col_count = lax.axis_size("col")
    operators = broadcast(bank[0, 0], owner)
    row_ids = lax.axis_index("row") * cell_rows + jnp.arange(cell_rows, dtype=jnp.int32)
    col_ids = lax.axis_index("col") * cell_cols + jnp.arange(cell_cols, dtype=jnp.int32)
    flat_ids = row_ids[:, None] * (cell_cols * col_count) + col_ids[None, :]
    port_hits = (flat_ids[:, :, None] == port_cell[None, None, :]).astype(jnp.float32)
    source = port_hits[..., None] * excite[None, None]
    kinds = cell_type[:, :, None, None]
    traces = incoming
    outgoing = incoming
    for sweep_id in range(SWEEPS):
        rows = traces.reshape(cell_rows * cell_cols * port_count, order)
        products = [
            jnp.dot(rows, operators[k], preferred_element_type=jnp.float32).reshape(
                cell_rows, cell_cols, port_count, order
            )
            for k in range(TYPES)
        ]
        chosen = products[0]
        for k in range(1, TYPES):
            chosen = jnp.where(kinds == k, products[k], chosen)
        outgoing = (chosen + source).astype(jnp.bfloat16)
        if sweep_id + 1 < SWEEPS:
            traces = pass_traces(outgoing)
    return outgoing


def solution(mesh):
    in_specs = (
        P("row", "col", None, None),
        P("row", "col"),
        P("row", "col", None, None),
        P(),
        P(),
        P(),
    )
    out_specs = P("row", "col", None, None)
    return jax.shard_map(local, mesh=mesh, in_specs=in_specs, out_specs=out_specs, check_vma=False)
```

```python
import jax
import jax.numpy as jnp
from jax import lax
from jax.sharding import PartitionSpec as P

TYPES = 2
SWEEPS = 3


def with_halo(block, sides, width):
    for axis, dim in sides:
        count = lax.axis_size(axis)
        forward = [(i, i + 1) for i in range(count - 1)]
        backward = [(target, source) for source, target in forward]
        low = lax.ppermute(
            lax.slice_in_dim(block, block.shape[dim] - width, None, axis=dim), axis, forward
        )
        high = lax.ppermute(lax.slice_in_dim(block, 0, width, axis=dim), axis, backward)
        block = jnp.concatenate([low, block, high], axis=dim)
    return block


def pass_traces(outgoing):
    face_len = outgoing.shape[-1] // 4
    west_face = outgoing[..., :face_len]
    east_face = outgoing[..., face_len : 2 * face_len]
    north_face = outgoing[..., 2 * face_len : 3 * face_len]
    south_face = outgoing[..., 3 * face_len :]
    side_send = jnp.stack([west_face[:, 0], east_face[:, -1]], axis=1)
    side_got = with_halo(side_send, (("col", 1),), 1)
    new_west = jnp.concatenate([side_got[:, 0][:, None], east_face[:, :-1]], axis=1)
    new_east = jnp.concatenate([west_face[:, 1:], side_got[:, 3][:, None]], axis=1)
    end_send = jnp.stack([north_face[0], south_face[-1]], axis=0)
    end_got = with_halo(end_send, (("row", 0),), 1)
    new_north = jnp.concatenate([end_got[0][None], south_face[:-1]], axis=0)
    new_south = jnp.concatenate([north_face[1:], end_got[3][None]], axis=0)
    return jnp.concatenate([new_west, new_east, new_north, new_south], axis=-1)


def device_bits(axis):
    count = lax.axis_size(axis)
    bits = count.bit_length() - 1
    return bits if (1 << bits) == count else None


def swap(block, bit, col_bits):
    count = lax.axis_size("col") * lax.axis_size("row")
    pairs = [(i, i ^ (1 << bit)) for i in range(count)]
    return lax.ppermute(block, ("row", "col"), pairs)


def scatter_gather(block, owner, order, col_bits, me):
    done_mask = 0
    full = (1 << len(order)) - 1
    for bit in order:
        half = block.shape[1] // 2
        mine = ((me >> bit) & 1) == 1
        low, high = block[:, :half], block[:, half:]
        keep = jnp.where(mine, high, low)
        give = jnp.where(mine, low, high)
        got = swap(give, bit, col_bits)
        outside = full & ~done_mask
        have = ((me ^ owner) & outside) == 0
        block = jnp.where(have[:, None, None], keep, got)
        done_mask |= 1 << bit
    for bit in reversed(order):
        mine = ((me >> bit) & 1) == 1
        got = swap(block, bit, col_bits)
        block = jnp.where(
            mine, jnp.concatenate([got, block], axis=1), jnp.concatenate([block, got], axis=1)
        )
    return block


def broadcast_parts(own_operator, owner):
    col_bits = device_bits("col")
    row_bits = device_bits("row")
    me = lax.axis_index("row") * lax.axis_size("col") + lax.axis_index("col")
    stacked = jnp.stack([own_operator] * TYPES, axis=0)
    order_len = None if col_bits is None or row_bits is None else col_bits + row_bits
    if order_len is None or row_bits < 1 or col_bits < 1 or (own_operator.shape[0] >> order_len) < 8:
        mask = (me == owner)[:, None, None]
        return [lax.psum(jnp.where(mask, stacked, jnp.zeros_like(stacked)), ("row", "col"))]
    core = col_bits
    middle = list(range(col_bits - 1)) + list(range(col_bits + 1, col_bits + row_bits))
    last = [col_bits - 1]
    streams = max(1, min(3, len(middle)))
    width = own_operator.shape[1]
    unit = width // 128
    sizes = [unit // streams + (1 if s < unit % streams else 0) for s in range(streams)]
    parts = []
    offset = 0
    for s in range(streams):
        cols = sizes[s] * 128
        rotated = middle[s:] + middle[:s]
        order = [core] + rotated + last
        piece = stacked[:, :, offset : offset + cols]
        parts.append(scatter_gather(piece, owner, order, col_bits, me))
        offset += cols
    return parts


def local(incoming, cell_type, bank, owner, port_cell, excite):
    cell_rows, cell_cols, port_count, order = incoming.shape
    col_count = lax.axis_size("col")
    parts = broadcast_parts(bank[0, 0], owner)
    row_ids = lax.axis_index("row") * cell_rows + jnp.arange(cell_rows, dtype=jnp.int32)
    col_ids = lax.axis_index("col") * cell_cols + jnp.arange(cell_cols, dtype=jnp.int32)
    flat_ids = row_ids[:, None] * (cell_cols * col_count) + col_ids[None, :]
    port_hits = (flat_ids[:, :, None] == port_cell[None, None, :]).astype(jnp.float32)
    source = port_hits[..., None] * excite[None, None]
    kinds = cell_type[:, :, None, None]
    traces = incoming
    outgoing = incoming
    for sweep_id in range(SWEEPS):
        rows = traces.reshape(cell_rows * cell_cols * port_count, order)
        products = [
            jnp.concatenate(
                [jnp.dot(rows, part[k], preferred_element_type=jnp.float32) for part in parts], axis=-1
            ).reshape(cell_rows, cell_cols, port_count, order)
            for k in range(TYPES)
        ]
        chosen = products[0]
        for k in range(1, TYPES):
            chosen = jnp.where(kinds == k, products[k], chosen)
        outgoing = (chosen + source).astype(jnp.bfloat16)
        if sweep_id + 1 < SWEEPS:
            traces = pass_traces(outgoing)
    return outgoing


def solution(mesh):
    in_specs = (
        P("row", "col", None, None),
        P("row", "col"),
        P("row", "col", None, None),
        P(),
        P(),
        P(),
    )
    out_specs = P("row", "col", None, None)
    return jax.shard_map(local, mesh=mesh, in_specs=in_specs, out_specs=out_specs, check_vma=False)
```

```python
import jax
import jax.numpy as jnp
from jax import lax
from jax.sharding import PartitionSpec as P

TYPES = 2
SWEEPS = 3


def with_halo(block, sides, width):
    for axis, dim in sides:
        count = lax.axis_size(axis)
        forward = [(i, i + 1) for i in range(count - 1)]
        backward = [(target, source) for source, target in forward]
        low = lax.ppermute(
            lax.slice_in_dim(block, block.shape[dim] - width, None, axis=dim), axis, forward
        )
        high = lax.ppermute(lax.slice_in_dim(block, 0, width, axis=dim), axis, backward)
        block = jnp.concatenate([low, block, high], axis=dim)
    return block


def pass_traces(outgoing):
    face_len = outgoing.shape[-1] // 4
    west_face = outgoing[..., :face_len]
    east_face = outgoing[..., face_len : 2 * face_len]
    north_face = outgoing[..., 2 * face_len : 3 * face_len]
    south_face = outgoing[..., 3 * face_len :]
    side_send = jnp.stack([west_face[:, 0], east_face[:, -1]], axis=1)
    side_got = with_halo(side_send, (("col", 1),), 1)
    new_west = jnp.concatenate([side_got[:, 0][:, None], east_face[:, :-1]], axis=1)
    new_east = jnp.concatenate([west_face[:, 1:], side_got[:, 3][:, None]], axis=1)
    end_send = jnp.stack([north_face[0], south_face[-1]], axis=0)
    end_got = with_halo(end_send, (("row", 0),), 1)
    new_north = jnp.concatenate([end_got[0][None], south_face[:-1]], axis=0)
    new_south = jnp.concatenate([north_face[1:], end_got[3][None]], axis=0)
    return jnp.concatenate([new_west, new_east, new_north, new_south], axis=-1)


def device_bits(axis):
    count = lax.axis_size(axis)
    bits = count.bit_length() - 1
    return bits if (1 << bits) == count else None


def swap(block, bit, col_bits):
    count = lax.axis_size("col") * lax.axis_size("row")
    pairs = [(i, i ^ (1 << bit)) for i in range(count)]
    return lax.ppermute(block, ("row", "col"), pairs)


def scatter_gather(block, owner, order, col_bits, me):
    done_mask = 0
    full = (1 << len(order)) - 1
    for bit in order:
        half = block.shape[1] // 2
        mine = ((me >> bit) & 1) == 1
        low, high = block[:, :half], block[:, half:]
        keep = jnp.where(mine, high, low)
        give = jnp.where(mine, low, high)
        got = swap(give, bit, col_bits)
        outside = full & ~done_mask
        have = ((me ^ owner) & outside) == 0
        block = jnp.where(have[:, None, None], keep, got)
        done_mask |= 1 << bit
    for bit in reversed(order):
        mine = ((me >> bit) & 1) == 1
        got = swap(block, bit, col_bits)
        block = jnp.where(
            mine, jnp.concatenate([got, block], axis=1), jnp.concatenate([block, got], axis=1)
        )
    return block


def broadcast_parts(own_operator, owner):
    col_bits = device_bits("col")
    row_bits = device_bits("row")
    me = lax.axis_index("row") * lax.axis_size("col") + lax.axis_index("col")
    stacked = jnp.stack([own_operator] * TYPES, axis=0)
    order_len = None if col_bits is None or row_bits is None else col_bits + row_bits
    if order_len is None or row_bits < 1 or col_bits < 1 or (own_operator.shape[0] >> order_len) < 8:
        mask = (me == owner)[:, None, None]
        return [lax.psum(jnp.where(mask, stacked, jnp.zeros_like(stacked)), ("row", "col"))]
    core = col_bits
    middle = list(range(col_bits - 1)) + list(range(col_bits + 1, col_bits + row_bits))
    last = [col_bits - 1]
    streams = max(1, min(3, len(middle)))
    width = own_operator.shape[1]
    unit = width // 128
    sizes = [unit // streams + (1 if s < unit % streams else 0) for s in range(streams)]
    parts = []
    offset = 0
    for s in range(streams):
        cols = sizes[s] * 128
        rotated = middle[s:] + middle[:s]
        order = [core] + rotated + last
        piece = stacked[:, :, offset : offset + cols]
        parts.append(scatter_gather(piece, owner, order, col_bits, me))
        offset += cols
    return parts


def sweep(traces, kinds, ids, parts, port_cell, excite):
    count, port_count, order = traces.shape
    rows = traces.reshape(count * port_count, order)
    products = [
        jnp.concatenate(
            [jnp.dot(rows, part[k], preferred_element_type=jnp.float32) for part in parts], axis=-1
        ).reshape(count, port_count, order)
        for k in range(TYPES)
    ]
    chosen = products[0]
    for k in range(1, TYPES):
        chosen = jnp.where((kinds == k)[:, None, None], products[k], chosen)
    port_hits = (ids[:, None] == port_cell[None, :]).astype(jnp.float32)
    source = port_hits[..., None] * excite[None]
    return (chosen + source).astype(jnp.bfloat16)


def shift(block, axis, step):
    count = lax.axis_size(axis)
    if step > 0:
        pairs = [(i, i + 1) for i in range(count - 1)]
    else:
        pairs = [(i + 1, i) for i in range(count - 1)]
    return lax.ppermute(block, axis, pairs)


def local(incoming, cell_type, bank, owner, port_cell, excite):
    cell_rows, cell_cols, port_count, order = incoming.shape
    col_count = lax.axis_size("col")
    row_count = lax.axis_size("row")
    row_at = lax.axis_index("row")
    col_at = lax.axis_index("col")
    width = cell_cols * col_count
    face = order // 4
    tagged = jnp.concatenate(
        [incoming, jnp.broadcast_to(cell_type.astype(incoming.dtype)[:, :, None, None], (cell_rows, cell_cols, port_count, 128))],
        axis=-1,
    )
    from_west = shift(tagged[:, -1], "col", 1)
    from_east = shift(tagged[:, 0], "col", -1)
    from_north = shift(tagged[-1], "row", 1)
    from_south = shift(tagged[0], "row", -1)
    parts = broadcast_parts(bank[0, 0], owner)
    row_ids = row_at * cell_rows + jnp.arange(cell_rows, dtype=jnp.int32)
    col_ids = col_at * cell_cols + jnp.arange(cell_cols, dtype=jnp.int32)
    flat_ids = (row_ids[:, None] * width + col_ids[None, :]).reshape(-1)
    ghost = jnp.concatenate([from_west, from_east, from_north, from_south], axis=0)
    ghost_ids = jnp.concatenate(
        [
            row_ids * width + col_at * cell_cols - 1,
            row_ids * width + (col_at + 1) * cell_cols,
            (row_at * cell_rows - 1) * width + col_ids,
            ((row_at + 1) * cell_rows) * width + col_ids,
        ]
    )
    cell_count = cell_rows * cell_cols
    all_traces = jnp.concatenate([incoming.reshape(cell_count, port_count, order), ghost[:, :, :order]], axis=0)
    all_kinds = jnp.concatenate([cell_type.reshape(-1), ghost[:, 0, order].astype(jnp.int32)])
    all_ids = jnp.concatenate([flat_ids, ghost_ids])
    first = sweep(all_traces, all_kinds, all_ids, parts, port_cell, excite)
    outgoing = first[:cell_count].reshape(cell_rows, cell_cols, port_count, order)
    ghost_out = first[cell_count:]
    zero = jnp.zeros_like(ghost_out[:cell_rows, :, :face])
    west_in = jnp.where(col_at > 0, ghost_out[:cell_rows, :, face : 2 * face], zero)
    east_in = jnp.where(col_at < col_count - 1, ghost_out[cell_rows : 2 * cell_rows, :, :face], zero)
    zero = jnp.zeros_like(ghost_out[:cell_cols, :, :face])
    at = 2 * cell_rows
    north_in = jnp.where(row_at > 0, ghost_out[at : at + cell_cols, :, 3 * face :], zero)
    south_in = jnp.where(
        row_at < row_count - 1, ghost_out[at + cell_cols : at + 2 * cell_cols, :, 2 * face : 3 * face], zero
    )
    traces = assemble(outgoing, west_in, east_in, north_in, south_in)
    kinds = cell_type.reshape(-1)
    for sweep_id in range(1, SWEEPS):
        outgoing = sweep(traces.reshape(cell_count, port_count, order), kinds, flat_ids, parts, port_cell, excite)
        outgoing = outgoing.reshape(cell_rows, cell_cols, port_count, order)
        if sweep_id + 1 < SWEEPS:
            traces = pass_traces(outgoing)
    return outgoing


def assemble(outgoing, west_in, east_in, north_in, south_in):
    face_len = outgoing.shape[-1] // 4
    west_face = outgoing[..., :face_len]
    east_face = outgoing[..., face_len : 2 * face_len]
    north_face = outgoing[..., 2 * face_len : 3 * face_len]
    south_face = outgoing[..., 3 * face_len :]
    new_west = jnp.concatenate([west_in[:, None], east_face[:, :-1]], axis=1)
    new_east = jnp.concatenate([west_face[:, 1:], east_in[:, None]], axis=1)
    new_north = jnp.concatenate([north_in[None], south_face[:-1]], axis=0)
    new_south = jnp.concatenate([north_face[1:], south_in[None]], axis=0)
    return jnp.concatenate([new_west, new_east, new_north, new_south], axis=-1)


def solution(mesh):
    in_specs = (
        P("row", "col", None, None),
        P("row", "col"),
        P("row", "col", None, None),
        P(),
        P(),
        P(),
    )
    out_specs = P("row", "col", None, None)
    return jax.shard_map(local, mesh=mesh, in_specs=in_specs, out_specs=out_specs, check_vma=False)
```

```python
import jax
import jax.numpy as jnp
from jax import lax
from jax.sharding import PartitionSpec as P

TYPES = 2
SWEEPS = 3


def with_halo(block, sides, width):
    for axis, dim in sides:
        count = lax.axis_size(axis)
        forward = [(i, i + 1) for i in range(count - 1)]
        backward = [(target, source) for source, target in forward]
        low = lax.ppermute(
            lax.slice_in_dim(block, block.shape[dim] - width, None, axis=dim), axis, forward
        )
        high = lax.ppermute(lax.slice_in_dim(block, 0, width, axis=dim), axis, backward)
        block = jnp.concatenate([low, block, high], axis=dim)
    return block


def pass_traces(outgoing):
    face_len = outgoing.shape[-1] // 4
    west_face = outgoing[..., :face_len]
    east_face = outgoing[..., face_len : 2 * face_len]
    north_face = outgoing[..., 2 * face_len : 3 * face_len]
    south_face = outgoing[..., 3 * face_len :]
    side_send = jnp.stack([west_face[:, 0], east_face[:, -1]], axis=1)
    side_got = with_halo(side_send, (("col", 1),), 1)
    new_west = jnp.concatenate([side_got[:, 0][:, None], east_face[:, :-1]], axis=1)
    new_east = jnp.concatenate([west_face[:, 1:], side_got[:, 3][:, None]], axis=1)
    end_send = jnp.stack([north_face[0], south_face[-1]], axis=0)
    end_got = with_halo(end_send, (("row", 0),), 1)
    new_north = jnp.concatenate([end_got[0][None], south_face[:-1]], axis=0)
    new_south = jnp.concatenate([north_face[1:], end_got[3][None]], axis=0)
    return jnp.concatenate([new_west, new_east, new_north, new_south], axis=-1)


def device_bits(axis):
    count = lax.axis_size(axis)
    bits = count.bit_length() - 1
    return bits if (1 << bits) == count else None


def swap(block, bit, col_bits):
    count = lax.axis_size("col") * lax.axis_size("row")
    pairs = [(i, i ^ (1 << bit)) for i in range(count)]
    return lax.ppermute(block, ("row", "col"), pairs)


def scatter_gather(block, owner, order, col_bits, me, tie):
    done_mask = 0
    full = (1 << len(order)) - 1
    for bit in order:
        half = block.shape[1] // 2
        mine = ((me >> bit) & 1) == 1
        low, high = block[:, :half], block[:, half:]
        keep = jnp.where(mine, high, low)
        give = jnp.where(mine, low, high)
        got = swap(give, bit, col_bits)
        outside = full & ~done_mask
        have = ((me ^ owner) & outside) == 0
        block = jnp.where(have[:, None, None], keep, got)
        done_mask |= 1 << bit
    block, tie = lax.optimization_barrier((block, tie))
    for bit in reversed(order):
        mine = ((me >> bit) & 1) == 1
        got = swap(block, bit, col_bits)
        block = jnp.where(
            mine, jnp.concatenate([got, block], axis=1), jnp.concatenate([block, got], axis=1)
        )
    return block, tie


def broadcast_parts(own_operator, owner, tie):
    col_bits = device_bits("col")
    row_bits = device_bits("row")
    me = lax.axis_index("row") * lax.axis_size("col") + lax.axis_index("col")
    stacked = jnp.stack([own_operator] * TYPES, axis=0)
    order_len = None if col_bits is None or row_bits is None else col_bits + row_bits
    if order_len is None or row_bits < 1 or col_bits < 1 or (own_operator.shape[0] >> order_len) < 8:
        mask = (me == owner)[:, None, None]
        return [lax.psum(jnp.where(mask, stacked, jnp.zeros_like(stacked)), ("row", "col"))], tie
    core = col_bits
    middle = list(range(col_bits - 1)) + list(range(col_bits + 1, col_bits + row_bits))
    last = [col_bits - 1]
    streams = max(1, min(3, len(middle)))
    width = own_operator.shape[1]
    unit = width // 128
    sizes = [unit // streams + (1 if s < unit % streams else 0) for s in range(streams)]
    parts = []
    offset = 0
    for s in range(streams):
        cols = sizes[s] * 128
        rotated = middle[s:] + middle[:s]
        order = [core] + rotated + last
        piece = stacked[:, :, offset : offset + cols]
        gathered, tie = scatter_gather(piece, owner, order, col_bits, me, tie)
        parts.append(gathered)
        offset += cols
    return parts, tie


def sweep(traces, kinds, ids, parts, port_cell, excite):
    count, port_count, order = traces.shape
    rows = traces.reshape(count * port_count, order)
    products = [
        jnp.concatenate(
            [jnp.dot(rows, part[k], preferred_element_type=jnp.float32) for part in parts], axis=-1
        ).reshape(count, port_count, order)
        for k in range(TYPES)
    ]
    chosen = products[0]
    for k in range(1, TYPES):
        chosen = jnp.where((kinds == k)[:, None, None], products[k], chosen)
    port_hits = (ids[:, None] == port_cell[None, :]).astype(jnp.float32)
    source = port_hits[..., None] * excite[None]
    return (chosen + source).astype(jnp.bfloat16)


def shift(block, axis, step):
    count = lax.axis_size(axis)
    if step > 0:
        pairs = [(i, i + 1) for i in range(count - 1)]
    else:
        pairs = [(i + 1, i) for i in range(count - 1)]
    return lax.ppermute(block, axis, pairs)


def local(incoming, cell_type, bank, owner, port_cell, excite):
    cell_rows, cell_cols, port_count, order = incoming.shape
    col_count = lax.axis_size("col")
    row_count = lax.axis_size("row")
    row_at = lax.axis_index("row")
    col_at = lax.axis_index("col")
    width = cell_cols * col_count
    face = order // 4
    tagged = jnp.concatenate(
        [incoming, jnp.broadcast_to(cell_type.astype(incoming.dtype)[:, :, None, None], (cell_rows, cell_cols, port_count, 128))],
        axis=-1,
    )
    parts, tagged = broadcast_parts(bank[0, 0], owner, tagged)
    from_west = shift(tagged[:, -1], "col", 1)
    from_east = shift(tagged[:, 0], "col", -1)
    from_north = shift(tagged[-1], "row", 1)
    from_south = shift(tagged[0], "row", -1)
    row_ids = row_at * cell_rows + jnp.arange(cell_rows, dtype=jnp.int32)
    col_ids = col_at * cell_cols + jnp.arange(cell_cols, dtype=jnp.int32)
    flat_ids = (row_ids[:, None] * width + col_ids[None, :]).reshape(-1)
    ghost = jnp.concatenate([from_west, from_east, from_north, from_south], axis=0)
    ghost_ids = jnp.concatenate(
        [
            row_ids * width + col_at * cell_cols - 1,
            row_ids * width + (col_at + 1) * cell_cols,
            (row_at * cell_rows - 1) * width + col_ids,
            ((row_at + 1) * cell_rows) * width + col_ids,
        ]
    )
    cell_count = cell_rows * cell_cols
    all_traces = jnp.concatenate([incoming.reshape(cell_count, port_count, order), ghost[:, :, :order]], axis=0)
    all_kinds = jnp.concatenate([cell_type.reshape(-1), ghost[:, 0, order].astype(jnp.int32)])
    all_ids = jnp.concatenate([flat_ids, ghost_ids])
    first = sweep(all_traces, all_kinds, all_ids, parts, port_cell, excite)
    outgoing = first[:cell_count].reshape(cell_rows, cell_cols, port_count, order)
    ghost_out = first[cell_count:]
    zero = jnp.zeros_like(ghost_out[:cell_rows, :, :face])
    west_in = jnp.where(col_at > 0, ghost_out[:cell_rows, :, face : 2 * face], zero)
    east_in = jnp.where(col_at < col_count - 1, ghost_out[cell_rows : 2 * cell_rows, :, :face], zero)
    zero = jnp.zeros_like(ghost_out[:cell_cols, :, :face])
    at = 2 * cell_rows
    north_in = jnp.where(row_at > 0, ghost_out[at : at + cell_cols, :, 3 * face :], zero)
    south_in = jnp.where(
        row_at < row_count - 1, ghost_out[at + cell_cols : at + 2 * cell_cols, :, 2 * face : 3 * face], zero
    )
    traces = assemble(outgoing, west_in, east_in, north_in, south_in)
    kinds = cell_type.reshape(-1)
    for sweep_id in range(1, SWEEPS):
        outgoing = sweep(traces.reshape(cell_count, port_count, order), kinds, flat_ids, parts, port_cell, excite)
        outgoing = outgoing.reshape(cell_rows, cell_cols, port_count, order)
        if sweep_id + 1 < SWEEPS:
            traces = pass_traces(outgoing)
    return outgoing


def assemble(outgoing, west_in, east_in, north_in, south_in):
    face_len = outgoing.shape[-1] // 4
    west_face = outgoing[..., :face_len]
    east_face = outgoing[..., face_len : 2 * face_len]
    north_face = outgoing[..., 2 * face_len : 3 * face_len]
    south_face = outgoing[..., 3 * face_len :]
    new_west = jnp.concatenate([west_in[:, None], east_face[:, :-1]], axis=1)
    new_east = jnp.concatenate([west_face[:, 1:], east_in[:, None]], axis=1)
    new_north = jnp.concatenate([north_in[None], south_face[:-1]], axis=0)
    new_south = jnp.concatenate([north_face[1:], south_in[None]], axis=0)
    return jnp.concatenate([new_west, new_east, new_north, new_south], axis=-1)


def solution(mesh):
    in_specs = (
        P("row", "col", None, None),
        P("row", "col"),
        P("row", "col", None, None),
        P(),
        P(),
        P(),
    )
    out_specs = P("row", "col", None, None)
    return jax.shard_map(local, mesh=mesh, in_specs=in_specs, out_specs=out_specs, check_vma=False)
```

```python
import jax
import jax.numpy as jnp
from jax import lax
from jax.sharding import PartitionSpec as P

TYPES = 2
SWEEPS = 3


def with_halo(block, sides, width):
    for axis, dim in sides:
        count = lax.axis_size(axis)
        forward = [(i, i + 1) for i in range(count - 1)]
        backward = [(target, source) for source, target in forward]
        low = lax.ppermute(
            lax.slice_in_dim(block, block.shape[dim] - width, None, axis=dim), axis, forward
        )
        high = lax.ppermute(lax.slice_in_dim(block, 0, width, axis=dim), axis, backward)
        block = jnp.concatenate([low, block, high], axis=dim)
    return block


def pass_traces(outgoing):
    face_len = outgoing.shape[-1] // 4
    west_face = outgoing[..., :face_len]
    east_face = outgoing[..., face_len : 2 * face_len]
    north_face = outgoing[..., 2 * face_len : 3 * face_len]
    south_face = outgoing[..., 3 * face_len :]
    side_send = jnp.stack([west_face[:, 0], east_face[:, -1]], axis=1)
    side_got = with_halo(side_send, (("col", 1),), 1)
    new_west = jnp.concatenate([side_got[:, 0][:, None], east_face[:, :-1]], axis=1)
    new_east = jnp.concatenate([west_face[:, 1:], side_got[:, 3][:, None]], axis=1)
    end_send = jnp.stack([north_face[0], south_face[-1]], axis=0)
    end_got = with_halo(end_send, (("row", 0),), 1)
    new_north = jnp.concatenate([end_got[0][None], south_face[:-1]], axis=0)
    new_south = jnp.concatenate([north_face[1:], end_got[3][None]], axis=0)
    return jnp.concatenate([new_west, new_east, new_north, new_south], axis=-1)


def device_bits(axis):
    count = lax.axis_size(axis)
    bits = count.bit_length() - 1
    return bits if (1 << bits) == count else None


def swap(block, bit, col_bits):
    count = lax.axis_size("col") * lax.axis_size("row")
    pairs = [(i, i ^ (1 << bit)) for i in range(count)]
    return lax.ppermute(block, ("row", "col"), pairs)


def scatter_gather(block, owner, order, col_bits, me, tie):
    done_mask = 0
    full = (1 << len(order)) - 1
    for step, bit in enumerate(order):
        if step == 0:
            half = block.shape[0] // 2
            mine = ((me >> bit) & 1) == 1
            keep = jnp.where(mine, block[half:], block[:half])
            give = jnp.where(mine, block[:half], block[half:])
            got = swap(give, bit, col_bits)
            have = ((me ^ owner) & full) == 0
            block = jnp.where(have[:, None, None], keep[None], got[None])
            done_mask |= 1 << bit
            continue
        half = block.shape[1] // 2
        mine = ((me >> bit) & 1) == 1
        low, high = block[:, :half], block[:, half:]
        keep = jnp.where(mine, high, low)
        give = jnp.where(mine, low, high)
        got = swap(give, bit, col_bits)
        outside = full & ~done_mask
        have = ((me ^ owner) & outside) == 0
        block = jnp.where(have[:, None, None], keep, got)
        done_mask |= 1 << bit
    block, tie = lax.optimization_barrier((block, tie))
    for bit in reversed(order):
        mine = ((me >> bit) & 1) == 1
        got = swap(block, bit, col_bits)
        block = jnp.where(
            mine, jnp.concatenate([got, block], axis=1), jnp.concatenate([block, got], axis=1)
        )
    return block, tie


def broadcast_parts(own_operator, owner, tie):
    col_bits = device_bits("col")
    row_bits = device_bits("row")
    me = lax.axis_index("row") * lax.axis_size("col") + lax.axis_index("col")
    stacked = jnp.stack([own_operator] * TYPES, axis=0)
    order_len = None if col_bits is None or row_bits is None else col_bits + row_bits
    if order_len is None or row_bits < 1 or col_bits < 1 or (own_operator.shape[0] >> order_len) < 8:
        mask = (me == owner)[:, None, None]
        return [lax.psum(jnp.where(mask, stacked, jnp.zeros_like(stacked)), ("row", "col"))], tie
    core = col_bits
    middle = list(range(col_bits - 1)) + list(range(col_bits + 1, col_bits + row_bits))
    last = [col_bits - 1]
    streams = max(1, min(3, len(middle)))
    width = own_operator.shape[1]
    unit = width // 128
    sizes = [unit // streams + (1 if s < unit % streams else 0) for s in range(streams)]
    parts = []
    offset = 0
    for s in range(streams):
        cols = sizes[s] * 128
        rotated = middle[s:] + middle[:s]
        order = [core] + rotated + last
        piece = own_operator[:, offset : offset + cols]
        gathered, tie = scatter_gather(piece, owner, order, col_bits, me, tie)
        parts.append(gathered)
        offset += cols
    return parts, tie


def sweep(traces, kinds, ids, parts, port_cell, excite):
    count, port_count, order = traces.shape
    rows = traces.reshape(count * port_count, order)
    products = [
        jnp.concatenate(
            [jnp.dot(rows, part[k], preferred_element_type=jnp.float32) for part in parts], axis=-1
        ).reshape(count, port_count, order)
        for k in range(TYPES)
    ]
    chosen = products[0]
    for k in range(1, TYPES):
        chosen = jnp.where((kinds == k)[:, None, None], products[k], chosen)
    port_hits = (ids[:, None] == port_cell[None, :]).astype(jnp.float32)
    source = port_hits[..., None] * excite[None]
    return (chosen + source).astype(jnp.bfloat16)


def shift(block, axis, step):
    count = lax.axis_size(axis)
    if step > 0:
        pairs = [(i, i + 1) for i in range(count - 1)]
    else:
        pairs = [(i + 1, i) for i in range(count - 1)]
    return lax.ppermute(block, axis, pairs)


def local(incoming, cell_type, bank, owner, port_cell, excite):
    cell_rows, cell_cols, port_count, order = incoming.shape
    col_count = lax.axis_size("col")
    row_count = lax.axis_size("row")
    row_at = lax.axis_index("row")
    col_at = lax.axis_index("col")
    width = cell_cols * col_count
    face = order // 4
    tagged = jnp.concatenate(
        [incoming, jnp.broadcast_to(cell_type.astype(incoming.dtype)[:, :, None, None], (cell_rows, cell_cols, port_count, 128))],
        axis=-1,
    )
    parts, tagged = broadcast_parts(bank[0, 0], owner, tagged)
    from_west = shift(tagged[:, -1], "col", 1)
    from_east = shift(tagged[:, 0], "col", -1)
    from_north = shift(tagged[-1], "row", 1)
    from_south = shift(tagged[0], "row", -1)
    row_ids = row_at * cell_rows + jnp.arange(cell_rows, dtype=jnp.int32)
    col_ids = col_at * cell_cols + jnp.arange(cell_cols, dtype=jnp.int32)
    flat_ids = (row_ids[:, None] * width + col_ids[None, :]).reshape(-1)
    ghost = jnp.concatenate([from_west, from_east, from_north, from_south], axis=0)
    ghost_ids = jnp.concatenate(
        [
            row_ids * width + col_at * cell_cols - 1,
            row_ids * width + (col_at + 1) * cell_cols,
            (row_at * cell_rows - 1) * width + col_ids,
            ((row_at + 1) * cell_rows) * width + col_ids,
        ]
    )
    cell_count = cell_rows * cell_cols
    all_traces = jnp.concatenate([incoming.reshape(cell_count, port_count, order), ghost[:, :, :order]], axis=0)
    all_kinds = jnp.concatenate([cell_type.reshape(-1), ghost[:, 0, order].astype(jnp.int32)])
    all_ids = jnp.concatenate([flat_ids, ghost_ids])
    first = sweep(all_traces, all_kinds, all_ids, parts, port_cell, excite)
    outgoing = first[:cell_count].reshape(cell_rows, cell_cols, port_count, order)
    ghost_out = first[cell_count:]
    zero = jnp.zeros_like(ghost_out[:cell_rows, :, :face])
    west_in = jnp.where(col_at > 0, ghost_out[:cell_rows, :, face : 2 * face], zero)
    east_in = jnp.where(col_at < col_count - 1, ghost_out[cell_rows : 2 * cell_rows, :, :face], zero)
    zero = jnp.zeros_like(ghost_out[:cell_cols, :, :face])
    at = 2 * cell_rows
    north_in = jnp.where(row_at > 0, ghost_out[at : at + cell_cols, :, 3 * face :], zero)
    south_in = jnp.where(
        row_at < row_count - 1, ghost_out[at + cell_cols : at + 2 * cell_cols, :, 2 * face : 3 * face], zero
    )
    traces = assemble(outgoing, west_in, east_in, north_in, south_in)
    kinds = cell_type.reshape(-1)
    for sweep_id in range(1, SWEEPS):
        outgoing = sweep(traces.reshape(cell_count, port_count, order), kinds, flat_ids, parts, port_cell, excite)
        outgoing = outgoing.reshape(cell_rows, cell_cols, port_count, order)
        if sweep_id + 1 < SWEEPS:
            traces = pass_traces(outgoing)
    return outgoing


def assemble(outgoing, west_in, east_in, north_in, south_in):
    face_len = outgoing.shape[-1] // 4
    west_face = outgoing[..., :face_len]
    east_face = outgoing[..., face_len : 2 * face_len]
    north_face = outgoing[..., 2 * face_len : 3 * face_len]
    south_face = outgoing[..., 3 * face_len :]
    new_west = jnp.concatenate([west_in[:, None], east_face[:, :-1]], axis=1)
    new_east = jnp.concatenate([west_face[:, 1:], east_in[:, None]], axis=1)
    new_north = jnp.concatenate([north_in[None], south_face[:-1]], axis=0)
    new_south = jnp.concatenate([north_face[1:], south_in[None]], axis=0)
    return jnp.concatenate([new_west, new_east, new_north, new_south], axis=-1)


def solution(mesh):
    in_specs = (
        P("row", "col", None, None),
        P("row", "col"),
        P("row", "col", None, None),
        P(),
        P(),
        P(),
    )
    out_specs = P("row", "col", None, None)
    return jax.shard_map(local, mesh=mesh, in_specs=in_specs, out_specs=out_specs, check_vma=False)
```

```python
import jax
import jax.numpy as jnp
from jax import lax
from jax.sharding import PartitionSpec as P

TYPES = 2
SWEEPS = 3


def with_halo(block, sides, width):
    for axis, dim in sides:
        count = lax.axis_size(axis)
        forward = [(i, i + 1) for i in range(count - 1)]
        backward = [(target, source) for source, target in forward]
        low = lax.ppermute(
            lax.slice_in_dim(block, block.shape[dim] - width, None, axis=dim), axis, forward
        )
        high = lax.ppermute(lax.slice_in_dim(block, 0, width, axis=dim), axis, backward)
        block = jnp.concatenate([low, block, high], axis=dim)
    return block


def pass_traces(outgoing):
    face_len = outgoing.shape[-1] // 4
    west_face = outgoing[..., :face_len]
    east_face = outgoing[..., face_len : 2 * face_len]
    north_face = outgoing[..., 2 * face_len : 3 * face_len]
    south_face = outgoing[..., 3 * face_len :]
    side_send = jnp.stack([west_face[:, 0], east_face[:, -1]], axis=1)
    side_got = with_halo(side_send, (("col", 1),), 1)
    new_west = jnp.concatenate([side_got[:, 0][:, None], east_face[:, :-1]], axis=1)
    new_east = jnp.concatenate([west_face[:, 1:], side_got[:, 3][:, None]], axis=1)
    end_send = jnp.stack([north_face[0], south_face[-1]], axis=0)
    end_got = with_halo(end_send, (("row", 0),), 1)
    new_north = jnp.concatenate([end_got[0][None], south_face[:-1]], axis=0)
    new_south = jnp.concatenate([north_face[1:], end_got[3][None]], axis=0)
    return jnp.concatenate([new_west, new_east, new_north, new_south], axis=-1)


def device_bits(axis):
    count = lax.axis_size(axis)
    bits = count.bit_length() - 1
    return bits if (1 << bits) == count else None


def swap(block, bit, col_bits):
    count = lax.axis_size("col") * lax.axis_size("row")
    pairs = [(i, i ^ (1 << bit)) for i in range(count)]
    return lax.ppermute(block, ("row", "col"), pairs)


def scatter_gather(blocks, owner, orders, col_bits, me, tie):
    stages = len(orders[0])
    full = (1 << stages) - 1
    done_mask = [0] * len(blocks)
    for step in range(stages):
        gots, keeps = [], []
        for s, block in enumerate(blocks):
            bit = orders[s][step]
            mine = ((me >> bit) & 1) == 1
            if step == 0:
                half = block.shape[0] // 2
                keep = jnp.where(mine, block[half:], block[:half])[None]
                give = jnp.where(mine, block[:half], block[half:])
            else:
                half = block.shape[1] // 2
                keep = jnp.where(mine, block[:, half:], block[:, :half])
                give = jnp.where(mine, block[:, :half], block[:, half:])
            got = swap(give, bit, col_bits)
            keeps.append(keep)
            gots.append(got[None] if step == 0 else got)
        for s in range(len(blocks)):
            have = ((me ^ owner) & (full & ~done_mask[s])) == 0
            blocks[s] = jnp.where(have[:, None, None], keeps[s], gots[s])
            done_mask[s] |= 1 << orders[s][step]
        blocks = list(lax.optimization_barrier(tuple(blocks)))
    blocks, tie = lax.optimization_barrier((tuple(blocks), tie))
    blocks = list(blocks)
    for step in reversed(range(stages)):
        gots = [swap(block, orders[s][step], col_bits) for s, block in enumerate(blocks)]
        for s in range(len(blocks)):
            mine = ((me >> orders[s][step]) & 1) == 1
            blocks[s] = jnp.where(
                mine, jnp.concatenate([gots[s], blocks[s]], axis=1), jnp.concatenate([blocks[s], gots[s]], axis=1)
            )
    return blocks, tie


def broadcast_parts(own_operator, owner, tie):
    col_bits = device_bits("col")
    row_bits = device_bits("row")
    me = lax.axis_index("row") * lax.axis_size("col") + lax.axis_index("col")
    stacked = jnp.stack([own_operator] * TYPES, axis=0)
    order_len = None if col_bits is None or row_bits is None else col_bits + row_bits
    if order_len is None or row_bits < 1 or col_bits < 1 or (own_operator.shape[0] >> order_len) < 8:
        mask = (me == owner)[:, None, None]
        return [lax.psum(jnp.where(mask, stacked, jnp.zeros_like(stacked)), ("row", "col"))], tie
    core = col_bits
    middle = list(range(col_bits - 1)) + list(range(col_bits + 1, col_bits + row_bits))
    last = [col_bits - 1]
    streams = max(1, min(3, len(middle)))
    width = own_operator.shape[1]
    unit = width // 128
    sizes = [unit // streams + (1 if s < unit % streams else 0) for s in range(streams)]
    blocks, orders = [], []
    offset = 0
    for s in range(streams):
        cols = sizes[s] * 128
        orders.append([core] + middle[s:] + middle[:s] + last)
        blocks.append(own_operator[:, offset : offset + cols])
        offset += cols
    parts, tie = scatter_gather(blocks, owner, orders, col_bits, me, tie)
    return parts, tie


def sweep(traces, kinds, ids, parts, port_cell, excite):
    count, port_count, order = traces.shape
    rows = traces.reshape(count * port_count, order)
    products = [
        jnp.concatenate(
            [jnp.dot(rows, part[k], preferred_element_type=jnp.float32) for part in parts], axis=-1
        ).reshape(count, port_count, order)
        for k in range(TYPES)
    ]
    chosen = products[0]
    for k in range(1, TYPES):
        chosen = jnp.where((kinds == k)[:, None, None], products[k], chosen)
    port_hits = (ids[:, None] == port_cell[None, :]).astype(jnp.float32)
    source = port_hits[..., None] * excite[None]
    return (chosen + source).astype(jnp.bfloat16)


def shift(block, axis, step):
    count = lax.axis_size(axis)
    if step > 0:
        pairs = [(i, i + 1) for i in range(count - 1)]
    else:
        pairs = [(i + 1, i) for i in range(count - 1)]
    return lax.ppermute(block, axis, pairs)


def local(incoming, cell_type, bank, owner, port_cell, excite):
    cell_rows, cell_cols, port_count, order = incoming.shape
    col_count = lax.axis_size("col")
    row_count = lax.axis_size("row")
    row_at = lax.axis_index("row")
    col_at = lax.axis_index("col")
    width = cell_cols * col_count
    face = order // 4
    tagged = jnp.concatenate(
        [incoming, jnp.broadcast_to(cell_type.astype(incoming.dtype)[:, :, None, None], (cell_rows, cell_cols, port_count, 128))],
        axis=-1,
    )
    parts, tagged = broadcast_parts(bank[0, 0], owner, tagged)
    from_west = shift(tagged[:, -1], "col", 1)
    from_east = shift(tagged[:, 0], "col", -1)
    from_north = shift(tagged[-1], "row", 1)
    from_south = shift(tagged[0], "row", -1)
    row_ids = row_at * cell_rows + jnp.arange(cell_rows, dtype=jnp.int32)
    col_ids = col_at * cell_cols + jnp.arange(cell_cols, dtype=jnp.int32)
    flat_ids = (row_ids[:, None] * width + col_ids[None, :]).reshape(-1)
    ghost = jnp.concatenate([from_west, from_east, from_north, from_south], axis=0)
    ghost_ids = jnp.concatenate(
        [
            row_ids * width + col_at * cell_cols - 1,
            row_ids * width + (col_at + 1) * cell_cols,
            (row_at * cell_rows - 1) * width + col_ids,
            ((row_at + 1) * cell_rows) * width + col_ids,
        ]
    )
    cell_count = cell_rows * cell_cols
    all_traces = jnp.concatenate([incoming.reshape(cell_count, port_count, order), ghost[:, :, :order]], axis=0)
    all_kinds = jnp.concatenate([cell_type.reshape(-1), ghost[:, 0, order].astype(jnp.int32)])
    all_ids = jnp.concatenate([flat_ids, ghost_ids])
    first = sweep(all_traces, all_kinds, all_ids, parts, port_cell, excite)
    outgoing = first[:cell_count].reshape(cell_rows, cell_cols, port_count, order)
    ghost_out = first[cell_count:]
    zero = jnp.zeros_like(ghost_out[:cell_rows, :, :face])
    west_in = jnp.where(col_at > 0, ghost_out[:cell_rows, :, face : 2 * face], zero)
    east_in = jnp.where(col_at < col_count - 1, ghost_out[cell_rows : 2 * cell_rows, :, :face], zero)
    zero = jnp.zeros_like(ghost_out[:cell_cols, :, :face])
    at = 2 * cell_rows
    north_in = jnp.where(row_at > 0, ghost_out[at : at + cell_cols, :, 3 * face :], zero)
    south_in = jnp.where(
        row_at < row_count - 1, ghost_out[at + cell_cols : at + 2 * cell_cols, :, 2 * face : 3 * face], zero
    )
    traces = assemble(outgoing, west_in, east_in, north_in, south_in)
    kinds = cell_type.reshape(-1)
    for sweep_id in range(1, SWEEPS):
        outgoing = sweep(traces.reshape(cell_count, port_count, order), kinds, flat_ids, parts, port_cell, excite)
        outgoing = outgoing.reshape(cell_rows, cell_cols, port_count, order)
        if sweep_id + 1 < SWEEPS:
            traces = pass_traces(outgoing)
    return outgoing


def assemble(outgoing, west_in, east_in, north_in, south_in):
    face_len = outgoing.shape[-1] // 4
    west_face = outgoing[..., :face_len]
    east_face = outgoing[..., face_len : 2 * face_len]
    north_face = outgoing[..., 2 * face_len : 3 * face_len]
    south_face = outgoing[..., 3 * face_len :]
    new_west = jnp.concatenate([west_in[:, None], east_face[:, :-1]], axis=1)
    new_east = jnp.concatenate([west_face[:, 1:], east_in[:, None]], axis=1)
    new_north = jnp.concatenate([north_in[None], south_face[:-1]], axis=0)
    new_south = jnp.concatenate([north_face[1:], south_in[None]], axis=0)
    return jnp.concatenate([new_west, new_east, new_north, new_south], axis=-1)


def solution(mesh):
    in_specs = (
        P("row", "col", None, None),
        P("row", "col"),
        P("row", "col", None, None),
        P(),
        P(),
        P(),
    )
    out_specs = P("row", "col", None, None)
    return jax.shard_map(local, mesh=mesh, in_specs=in_specs, out_specs=out_specs, check_vma=False)
```

```python
import jax
import jax.numpy as jnp
from jax import lax
from jax.sharding import PartitionSpec as P

TYPES = 2
SWEEPS = 3


def with_halo(block, sides, width):
    for axis, dim in sides:
        count = lax.axis_size(axis)
        forward = [(i, i + 1) for i in range(count - 1)]
        backward = [(target, source) for source, target in forward]
        low = lax.ppermute(
            lax.slice_in_dim(block, block.shape[dim] - width, None, axis=dim), axis, forward
        )
        high = lax.ppermute(lax.slice_in_dim(block, 0, width, axis=dim), axis, backward)
        block = jnp.concatenate([low, block, high], axis=dim)
    return block


def pass_traces(outgoing):
    face_len = outgoing.shape[-1] // 4
    west_face = outgoing[..., :face_len]
    east_face = outgoing[..., face_len : 2 * face_len]
    north_face = outgoing[..., 2 * face_len : 3 * face_len]
    south_face = outgoing[..., 3 * face_len :]
    side_send = jnp.stack([west_face[:, 0], east_face[:, -1]], axis=1)
    side_got = with_halo(side_send, (("col", 1),), 1)
    new_west = jnp.concatenate([side_got[:, 0][:, None], east_face[:, :-1]], axis=1)
    new_east = jnp.concatenate([west_face[:, 1:], side_got[:, 3][:, None]], axis=1)
    end_send = jnp.stack([north_face[0], south_face[-1]], axis=0)
    end_got = with_halo(end_send, (("row", 0),), 1)
    new_north = jnp.concatenate([end_got[0][None], south_face[:-1]], axis=0)
    new_south = jnp.concatenate([north_face[1:], end_got[3][None]], axis=0)
    return jnp.concatenate([new_west, new_east, new_north, new_south], axis=-1)


def device_bits(axis):
    count = lax.axis_size(axis)
    bits = count.bit_length() - 1
    return bits if (1 << bits) == count else None


def swap(block, bit, col_bits):
    count = lax.axis_size("col") * lax.axis_size("row")
    pairs = [(i, i ^ (1 << bit)) for i in range(count)]
    return lax.ppermute(block, ("row", "col"), pairs)


def scatter_gather(blocks, owner, orders, col_bits, me, tie):
    stages = len(orders[0])
    full = (1 << stages) - 1
    done_mask = [0] * len(blocks)
    for step in range(stages):
        gots, keeps = [], []
        for s, block in enumerate(blocks):
            bit = orders[s][step]
            mine = ((me >> bit) & 1) == 1
            if step == 0:
                half = block.shape[0] // 2
                keep = jnp.where(mine, block[half:], block[:half])[None]
                give = jnp.where(mine, block[:half], block[half:])
            else:
                half = block.shape[1] // 2
                keep = jnp.where(mine, block[:, half:], block[:, :half])
                give = jnp.where(mine, block[:, :half], block[:, half:])
            got = swap(give, bit, col_bits)
            keeps.append(keep)
            gots.append(got[None] if step == 0 else got)
        for s in range(len(blocks)):
            have = ((me ^ owner) & (full & ~done_mask[s])) == 0
            blocks[s] = jnp.where(have[:, None, None], keeps[s], gots[s])
            done_mask[s] |= 1 << orders[s][step]
        blocks = list(lax.optimization_barrier(tuple(blocks)))
    blocks, tie = lax.optimization_barrier((tuple(blocks), tie))
    blocks = list(blocks)
    for step in reversed(range(stages)):
        gots = [swap(block, orders[s][step], col_bits) for s, block in enumerate(blocks)]
        for s in range(len(blocks)):
            mine = ((me >> orders[s][step]) & 1) == 1
            blocks[s] = jnp.where(
                mine, jnp.concatenate([gots[s], blocks[s]], axis=1), jnp.concatenate([blocks[s], gots[s]], axis=1)
            )
        if step == stages - 1:
            blocks = list(lax.optimization_barrier(tuple(blocks)))
    return blocks, tie


def broadcast_parts(own_operator, owner, tie):
    col_bits = device_bits("col")
    row_bits = device_bits("row")
    me = lax.axis_index("row") * lax.axis_size("col") + lax.axis_index("col")
    stacked = jnp.stack([own_operator] * TYPES, axis=0)
    order_len = None if col_bits is None or row_bits is None else col_bits + row_bits
    if order_len is None or row_bits < 1 or col_bits < 1 or (own_operator.shape[0] >> order_len) < 8:
        mask = (me == owner)[:, None, None]
        return [lax.psum(jnp.where(mask, stacked, jnp.zeros_like(stacked)), ("row", "col"))], tie
    core = col_bits
    middle = list(range(col_bits - 1)) + list(range(col_bits + 1, col_bits + row_bits))
    last = [col_bits - 1]
    streams = max(1, min(2, len(middle)))
    width = own_operator.shape[1]
    unit = width // 128
    sizes = [unit // streams + (1 if s < unit % streams else 0) for s in range(streams)]
    blocks, orders = [], []
    offset = 0
    for s in range(streams):
        cols = sizes[s] * 128
        orders.append([core] + middle[s:] + middle[:s] + last)
        blocks.append(own_operator[:, offset : offset + cols])
        offset += cols
    parts, tie = scatter_gather(blocks, owner, orders, col_bits, me, tie)
    return parts, tie


def sweep(traces, kinds, ids, parts, port_cell, excite):
    count, port_count, order = traces.shape
    rows = traces.reshape(count * port_count, order)
    products = [
        jnp.concatenate(
            [jnp.dot(rows, part[k], preferred_element_type=jnp.float32) for part in parts], axis=-1
        ).reshape(count, port_count, order)
        for k in range(TYPES)
    ]
    chosen = products[0]
    for k in range(1, TYPES):
        chosen = jnp.where((kinds == k)[:, None, None], products[k], chosen)
    port_hits = (ids[:, None] == port_cell[None, :]).astype(jnp.float32)
    source = port_hits[..., None] * excite[None]
    return (chosen + source).astype(jnp.bfloat16)


def shift(block, axis, step):
    count = lax.axis_size(axis)
    if step > 0:
        pairs = [(i, i + 1) for i in range(count - 1)]
    else:
        pairs = [(i + 1, i) for i in range(count - 1)]
    return lax.ppermute(block, axis, pairs)


def local(incoming, cell_type, bank, owner, port_cell, excite):
    cell_rows, cell_cols, port_count, order = incoming.shape
    col_count = lax.axis_size("col")
    row_count = lax.axis_size("row")
    row_at = lax.axis_index("row")
    col_at = lax.axis_index("col")
    width = cell_cols * col_count
    face = order // 4
    tagged = jnp.concatenate(
        [incoming, jnp.broadcast_to(cell_type.astype(incoming.dtype)[:, :, None, None], (cell_rows, cell_cols, port_count, 128))],
        axis=-1,
    )
    parts, tagged = broadcast_parts(bank[0, 0], owner, tagged)
    from_west = shift(tagged[:, -1], "col", 1)
    from_east = shift(tagged[:, 0], "col", -1)
    from_north = shift(tagged[-1], "row", 1)
    from_south = shift(tagged[0], "row", -1)
    row_ids = row_at * cell_rows + jnp.arange(cell_rows, dtype=jnp.int32)
    col_ids = col_at * cell_cols + jnp.arange(cell_cols, dtype=jnp.int32)
    flat_ids = (row_ids[:, None] * width + col_ids[None, :]).reshape(-1)
    ghost = jnp.concatenate([from_west, from_east, from_north, from_south], axis=0)
    ghost_ids = jnp.concatenate(
        [
            row_ids * width + col_at * cell_cols - 1,
            row_ids * width + (col_at + 1) * cell_cols,
            (row_at * cell_rows - 1) * width + col_ids,
            ((row_at + 1) * cell_rows) * width + col_ids,
        ]
    )
    cell_count = cell_rows * cell_cols
    all_traces = jnp.concatenate([incoming.reshape(cell_count, port_count, order), ghost[:, :, :order]], axis=0)
    all_kinds = jnp.concatenate([cell_type.reshape(-1), ghost[:, 0, order].astype(jnp.int32)])
    all_ids = jnp.concatenate([flat_ids, ghost_ids])
    first = sweep(all_traces, all_kinds, all_ids, parts, port_cell, excite)
    outgoing = first[:cell_count].reshape(cell_rows, cell_cols, port_count, order)
    ghost_out = first[cell_count:]
    zero = jnp.zeros_like(ghost_out[:cell_rows, :, :face])
    west_in = jnp.where(col_at > 0, ghost_out[:cell_rows, :, face : 2 * face], zero)
    east_in = jnp.where(col_at < col_count - 1, ghost_out[cell_rows : 2 * cell_rows, :, :face], zero)
    zero = jnp.zeros_like(ghost_out[:cell_cols, :, :face])
    at = 2 * cell_rows
    north_in = jnp.where(row_at > 0, ghost_out[at : at + cell_cols, :, 3 * face :], zero)
    south_in = jnp.where(
        row_at < row_count - 1, ghost_out[at + cell_cols : at + 2 * cell_cols, :, 2 * face : 3 * face], zero
    )
    traces = assemble(outgoing, west_in, east_in, north_in, south_in)
    kinds = cell_type.reshape(-1)
    for sweep_id in range(1, SWEEPS):
        outgoing = sweep(traces.reshape(cell_count, port_count, order), kinds, flat_ids, parts, port_cell, excite)
        outgoing = outgoing.reshape(cell_rows, cell_cols, port_count, order)
        if sweep_id + 1 < SWEEPS:
            traces = pass_traces(outgoing)
    return outgoing


def assemble(outgoing, west_in, east_in, north_in, south_in):
    face_len = outgoing.shape[-1] // 4
    west_face = outgoing[..., :face_len]
    east_face = outgoing[..., face_len : 2 * face_len]
    north_face = outgoing[..., 2 * face_len : 3 * face_len]
    south_face = outgoing[..., 3 * face_len :]
    new_west = jnp.concatenate([west_in[:, None], east_face[:, :-1]], axis=1)
    new_east = jnp.concatenate([west_face[:, 1:], east_in[:, None]], axis=1)
    new_north = jnp.concatenate([north_in[None], south_face[:-1]], axis=0)
    new_south = jnp.concatenate([north_face[1:], south_in[None]], axis=0)
    return jnp.concatenate([new_west, new_east, new_north, new_south], axis=-1)


def solution(mesh):
    in_specs = (
        P("row", "col", None, None),
        P("row", "col"),
        P("row", "col", None, None),
        P(),
        P(),
        P(),
    )
    out_specs = P("row", "col", None, None)
    return jax.shard_map(local, mesh=mesh, in_specs=in_specs, out_specs=out_specs, check_vma=False)
```

```python
import jax
import jax.numpy as jnp
from jax import lax
from jax.sharding import PartitionSpec as P

TYPES = 2
SWEEPS = 3


def with_halo(block, sides, width):
    for axis, dim in sides:
        count = lax.axis_size(axis)
        forward = [(i, i + 1) for i in range(count - 1)]
        backward = [(target, source) for source, target in forward]
        low = lax.ppermute(
            lax.slice_in_dim(block, block.shape[dim] - width, None, axis=dim), axis, forward
        )
        high = lax.ppermute(lax.slice_in_dim(block, 0, width, axis=dim), axis, backward)
        block = jnp.concatenate([low, block, high], axis=dim)
    return block


def pass_traces(outgoing):
    face_len = outgoing.shape[-1] // 4
    west_face = outgoing[..., :face_len]
    east_face = outgoing[..., face_len : 2 * face_len]
    north_face = outgoing[..., 2 * face_len : 3 * face_len]
    south_face = outgoing[..., 3 * face_len :]
    side_send = jnp.stack([west_face[:, 0], east_face[:, -1]], axis=1)
    side_got = with_halo(side_send, (("col", 1),), 1)
    new_west = jnp.concatenate([side_got[:, 0][:, None], east_face[:, :-1]], axis=1)
    new_east = jnp.concatenate([west_face[:, 1:], side_got[:, 3][:, None]], axis=1)
    end_send = jnp.stack([north_face[0], south_face[-1]], axis=0)
    end_got = with_halo(end_send, (("row", 0),), 1)
    new_north = jnp.concatenate([end_got[0][None], south_face[:-1]], axis=0)
    new_south = jnp.concatenate([north_face[1:], end_got[3][None]], axis=0)
    return jnp.concatenate([new_west, new_east, new_north, new_south], axis=-1)


def device_bits(axis):
    count = lax.axis_size(axis)
    bits = count.bit_length() - 1
    return bits if (1 << bits) == count else None


def swap(block, bits, core):
    count = lax.axis_size("col") * lax.axis_size("row")
    pairs = [(i, i ^ (1 << bits[(i >> core) & 1])) for i in range(count)]
    return lax.ppermute(block, ("row", "col"), pairs)


def scatter_gather(blocks, owner, orders, core, me, tie):
    stages = len(orders[0][0])
    full = (1 << stages) - 1
    my_core = (me >> core) & 1
    done_mask = [[0, 0] for _ in blocks]

    def pick(pair):
        return jnp.where(my_core == 1, pair[1], pair[0])

    for step in range(stages):
        gots, keeps = [], []
        for s, block in enumerate(blocks):
            bits = (orders[s][0][step], orders[s][1][step])
            mine = ((me >> pick(bits)) & 1) == 1
            if step == 0:
                half = block.shape[0] // 2
                keep = jnp.where(mine, block[half:], block[:half])[None]
                give = jnp.where(mine, block[:half], block[half:])
            else:
                half = block.shape[1] // 2
                keep = jnp.where(mine, block[:, half:], block[:, :half])
                give = jnp.where(mine, block[:, :half], block[:, half:])
            got = swap(give, bits, core)
            keeps.append(keep)
            gots.append(got[None] if step == 0 else got)
        for s in range(len(blocks)):
            outside = pick([full & ~done_mask[s][0], full & ~done_mask[s][1]])
            have = ((me ^ owner) & outside) == 0
            blocks[s] = jnp.where(have[:, None, None], keeps[s], gots[s])
            for c in range(2):
                done_mask[s][c] |= 1 << orders[s][c][step]
        blocks = list(lax.optimization_barrier(tuple(blocks)))
    blocks, tie = lax.optimization_barrier((tuple(blocks), tie))
    blocks = list(blocks)
    for step in reversed(range(stages)):
        gots = []
        for s, block in enumerate(blocks):
            gots.append(swap(block, (orders[s][0][step], orders[s][1][step]), core))
        for s in range(len(blocks)):
            mine = ((me >> pick((orders[s][0][step], orders[s][1][step]))) & 1) == 1
            blocks[s] = jnp.where(
                mine, jnp.concatenate([gots[s], blocks[s]], axis=1), jnp.concatenate([blocks[s], gots[s]], axis=1)
            )
        if step == stages - 1:
            blocks = list(lax.optimization_barrier(tuple(blocks)))
    return blocks, tie


def broadcast_parts(own_operator, owner, tie):
    col_bits = device_bits("col")
    row_bits = device_bits("row")
    me = lax.axis_index("row") * lax.axis_size("col") + lax.axis_index("col")
    stacked = jnp.stack([own_operator] * TYPES, axis=0)
    order_len = None if col_bits is None or row_bits is None else col_bits + row_bits
    if order_len is None or row_bits < 1 or col_bits < 1 or (own_operator.shape[0] >> order_len) < 8:
        mask = (me == owner)[:, None, None]
        return [lax.psum(jnp.where(mask, stacked, jnp.zeros_like(stacked)), ("row", "col"))], tie
    core = col_bits
    middle = list(range(col_bits - 1)) + list(range(col_bits + 1, col_bits + row_bits))
    last = [col_bits - 1]
    streams = max(1, min(2, len(middle)))
    width = own_operator.shape[1]
    unit = width // 128
    sizes = [unit // streams + (1 if s < unit % streams else 0) for s in range(streams)]
    blocks, orders = [], []
    offset = 0
    for s in range(streams):
        cols = sizes[s] * 128
        pair = []
        for c in range(2):
            turn = (2 * s + c) % len(middle)
            pair.append([core] + middle[turn:] + middle[:turn] + last)
        orders.append(pair)
        blocks.append(own_operator[:, offset : offset + cols])
        offset += cols
    parts, tie = scatter_gather(blocks, owner, orders, core, me, tie)
    return parts, tie


def sweep(traces, kinds, ids, parts, port_cell, excite):
    count, port_count, order = traces.shape
    rows = traces.reshape(count * port_count, order)
    products = [
        jnp.concatenate(
            [jnp.dot(rows, part[k], preferred_element_type=jnp.float32) for part in parts], axis=-1
        ).reshape(count, port_count, order)
        for k in range(TYPES)
    ]
    chosen = products[0]
    for k in range(1, TYPES):
        chosen = jnp.where((kinds == k)[:, None, None], products[k], chosen)
    port_hits = (ids[:, None] == port_cell[None, :]).astype(jnp.float32)
    source = port_hits[..., None] * excite[None]
    return (chosen + source).astype(jnp.bfloat16)


def shift(block, axis, step):
    count = lax.axis_size(axis)
    if step > 0:
        pairs = [(i, i + 1) for i in range(count - 1)]
    else:
        pairs = [(i + 1, i) for i in range(count - 1)]
    return lax.ppermute(block, axis, pairs)


def local(incoming, cell_type, bank, owner, port_cell, excite):
    cell_rows, cell_cols, port_count, order = incoming.shape
    col_count = lax.axis_size("col")
    row_count = lax.axis_size("row")
    row_at = lax.axis_index("row")
    col_at = lax.axis_index("col")
    width = cell_cols * col_count
    face = order // 4
    tagged = jnp.concatenate(
        [incoming, jnp.broadcast_to(cell_type.astype(incoming.dtype)[:, :, None, None], (cell_rows, cell_cols, port_count, 128))],
        axis=-1,
    )
    parts, tagged = broadcast_parts(bank[0, 0], owner, tagged)
    from_west = shift(tagged[:, -1], "col", 1)
    from_east = shift(tagged[:, 0], "col", -1)
    from_north = shift(tagged[-1], "row", 1)
    from_south = shift(tagged[0], "row", -1)
    row_ids = row_at * cell_rows + jnp.arange(cell_rows, dtype=jnp.int32)
    col_ids = col_at * cell_cols + jnp.arange(cell_cols, dtype=jnp.int32)
    flat_ids = (row_ids[:, None] * width + col_ids[None, :]).reshape(-1)
    ghost = jnp.concatenate([from_west, from_east, from_north, from_south], axis=0)
    ghost_ids = jnp.concatenate(
        [
            row_ids * width + col_at * cell_cols - 1,
            row_ids * width + (col_at + 1) * cell_cols,
            (row_at * cell_rows - 1) * width + col_ids,
            ((row_at + 1) * cell_rows) * width + col_ids,
        ]
    )
    cell_count = cell_rows * cell_cols
    all_traces = jnp.concatenate([incoming.reshape(cell_count, port_count, order), ghost[:, :, :order]], axis=0)
    all_kinds = jnp.concatenate([cell_type.reshape(-1), ghost[:, 0, order].astype(jnp.int32)])
    all_ids = jnp.concatenate([flat_ids, ghost_ids])
    first = sweep(all_traces, all_kinds, all_ids, parts, port_cell, excite)
    outgoing = first[:cell_count].reshape(cell_rows, cell_cols, port_count, order)
    ghost_out = first[cell_count:]
    zero = jnp.zeros_like(ghost_out[:cell_rows, :, :face])
    west_in = jnp.where(col_at > 0, ghost_out[:cell_rows, :, face : 2 * face], zero)
    east_in = jnp.where(col_at < col_count - 1, ghost_out[cell_rows : 2 * cell_rows, :, :face], zero)
    zero = jnp.zeros_like(ghost_out[:cell_cols, :, :face])
    at = 2 * cell_rows
    north_in = jnp.where(row_at > 0, ghost_out[at : at + cell_cols, :, 3 * face :], zero)
    south_in = jnp.where(
        row_at < row_count - 1, ghost_out[at + cell_cols : at + 2 * cell_cols, :, 2 * face : 3 * face], zero
    )
    traces = assemble(outgoing, west_in, east_in, north_in, south_in)
    kinds = cell_type.reshape(-1)
    for sweep_id in range(1, SWEEPS):
        outgoing = sweep(traces.reshape(cell_count, port_count, order), kinds, flat_ids, parts, port_cell, excite)
        outgoing = outgoing.reshape(cell_rows, cell_cols, port_count, order)
        if sweep_id + 1 < SWEEPS:
            traces = pass_traces(outgoing)
    return outgoing


def assemble(outgoing, west_in, east_in, north_in, south_in):
    face_len = outgoing.shape[-1] // 4
    west_face = outgoing[..., :face_len]
    east_face = outgoing[..., face_len : 2 * face_len]
    north_face = outgoing[..., 2 * face_len : 3 * face_len]
    south_face = outgoing[..., 3 * face_len :]
    new_west = jnp.concatenate([west_in[:, None], east_face[:, :-1]], axis=1)
    new_east = jnp.concatenate([west_face[:, 1:], east_in[:, None]], axis=1)
    new_north = jnp.concatenate([north_in[None], south_face[:-1]], axis=0)
    new_south = jnp.concatenate([north_face[1:], south_in[None]], axis=0)
    return jnp.concatenate([new_west, new_east, new_north, new_south], axis=-1)


def solution(mesh):
    in_specs = (
        P("row", "col", None, None),
        P("row", "col"),
        P("row", "col", None, None),
        P(),
        P(),
        P(),
    )
    out_specs = P("row", "col", None, None)
    return jax.shard_map(local, mesh=mesh, in_specs=in_specs, out_specs=out_specs, check_vma=False)
```

```python
import jax
import jax.numpy as jnp
from jax import lax
from jax.sharding import PartitionSpec as P

TYPES = 2
SWEEPS = 3


def neighbours(send_low, send_high, axis):
    count = lax.axis_size(axis)
    if count % 2:
        forward = [(i, i + 1) for i in range(count - 1)]
        backward = [(i + 1, i) for i in range(count - 1)]
        return lax.ppermute(send_high, axis, forward), lax.ppermute(send_low, axis, backward)
    even = lax.axis_index(axis) % 2 == 0
    inner = lax.ppermute(jnp.where(even, send_high, send_low), axis, [(i, i ^ 1) for i in range(count)])
    outer_pairs = [p for i in range(1, count - 1, 2) for p in ((i, i + 1), (i + 1, i))]
    outer = lax.ppermute(jnp.where(even, send_low, send_high), axis, outer_pairs)
    return jnp.where(even, outer, inner), jnp.where(even, inner, outer)


def pass_traces(outgoing):
    face_len = outgoing.shape[-1] // 4
    west_face = outgoing[..., :face_len]
    east_face = outgoing[..., face_len : 2 * face_len]
    north_face = outgoing[..., 2 * face_len : 3 * face_len]
    south_face = outgoing[..., 3 * face_len :]
    west_in, east_in = neighbours(west_face[:, 0], east_face[:, -1], "col")
    new_west = jnp.concatenate([west_in[:, None], east_face[:, :-1]], axis=1)
    new_east = jnp.concatenate([west_face[:, 1:], east_in[:, None]], axis=1)
    north_in, south_in = neighbours(north_face[0], south_face[-1], "row")
    new_north = jnp.concatenate([north_in[None], south_face[:-1]], axis=0)
    new_south = jnp.concatenate([north_face[1:], south_in[None]], axis=0)
    return jnp.concatenate([new_west, new_east, new_north, new_south], axis=-1)


def device_bits(axis):
    count = lax.axis_size(axis)
    bits = count.bit_length() - 1
    return bits if (1 << bits) == count else None


def swap(block, bits, core):
    count = lax.axis_size("col") * lax.axis_size("row")
    pairs = [(i, i ^ (1 << bits[(i >> core) & 1])) for i in range(count)]
    return lax.ppermute(block, ("row", "col"), pairs)


def scatter_gather(blocks, owner, orders, core, me, tie):
    stages = len(orders[0][0])
    full = (1 << stages) - 1
    my_core = (me >> core) & 1
    done_mask = [[0, 0] for _ in blocks]

    def pick(pair):
        return jnp.where(my_core == 1, pair[1], pair[0])

    for step in range(stages):
        gots, keeps = [], []
        for s, block in enumerate(blocks):
            bits = (orders[s][0][step], orders[s][1][step])
            mine = ((me >> pick(bits)) & 1) == 1
            if step == 0:
                half = block.shape[0] // 2
                keep = jnp.where(mine, block[half:], block[:half])[None]
                give = jnp.where(mine, block[:half], block[half:])
            else:
                half = block.shape[1] // 2
                keep = jnp.where(mine, block[:, half:], block[:, :half])
                give = jnp.where(mine, block[:, :half], block[:, half:])
            got = swap(give, bits, core)
            keeps.append(keep)
            gots.append(got[None] if step == 0 else got)
        for s in range(len(blocks)):
            outside = pick([full & ~done_mask[s][0], full & ~done_mask[s][1]])
            have = ((me ^ owner) & outside) == 0
            blocks[s] = jnp.where(have[:, None, None], keeps[s], gots[s])
            for c in range(2):
                done_mask[s][c] |= 1 << orders[s][c][step]
        blocks = list(lax.optimization_barrier(tuple(blocks)))
    blocks, tie = lax.optimization_barrier((tuple(blocks), tie))
    blocks = list(blocks)
    for step in reversed(range(stages)):
        gots = []
        for s, block in enumerate(blocks):
            gots.append(swap(block, (orders[s][0][step], orders[s][1][step]), core))
        for s in range(len(blocks)):
            mine = ((me >> pick((orders[s][0][step], orders[s][1][step]))) & 1) == 1
            blocks[s] = jnp.where(
                mine, jnp.concatenate([gots[s], blocks[s]], axis=1), jnp.concatenate([blocks[s], gots[s]], axis=1)
            )
        if step == stages - 1:
            blocks = list(lax.optimization_barrier(tuple(blocks)))
    return blocks, tie


def broadcast_parts(own_operator, owner, tie):
    col_bits = device_bits("col")
    row_bits = device_bits("row")
    me = lax.axis_index("row") * lax.axis_size("col") + lax.axis_index("col")
    stacked = jnp.stack([own_operator] * TYPES, axis=0)
    order_len = None if col_bits is None or row_bits is None else col_bits + row_bits
    if order_len is None or row_bits < 1 or col_bits < 1 or (own_operator.shape[0] >> order_len) < 8:
        mask = (me == owner)[:, None, None]
        return [lax.psum(jnp.where(mask, stacked, jnp.zeros_like(stacked)), ("row", "col"))], tie
    core = col_bits
    middle = list(range(col_bits - 1)) + list(range(col_bits + 1, col_bits + row_bits))
    last = [col_bits - 1]
    streams = max(1, min(2, len(middle)))
    width = own_operator.shape[1]
    unit = width // 128
    sizes = [unit // streams + (1 if s < unit % streams else 0) for s in range(streams)]
    blocks, orders = [], []
    offset = 0
    for s in range(streams):
        cols = sizes[s] * 128
        pair = []
        for c in range(2):
            turn = (2 * s + c) % len(middle)
            pair.append([core] + middle[turn:] + middle[:turn] + last)
        orders.append(pair)
        blocks.append(own_operator[:, offset : offset + cols])
        offset += cols
    parts, tie = scatter_gather(blocks, owner, orders, core, me, tie)
    return parts, tie


def sweep(traces, kinds, ids, parts, port_cell, excite):
    count, port_count, order = traces.shape
    rows = traces.reshape(count * port_count, order)
    products = [
        jnp.concatenate(
            [jnp.dot(rows, part[k], preferred_element_type=jnp.float32) for part in parts], axis=-1
        ).reshape(count, port_count, order)
        for k in range(TYPES)
    ]
    chosen = products[0]
    for k in range(1, TYPES):
        chosen = jnp.where((kinds == k)[:, None, None], products[k], chosen)
    port_hits = (ids[:, None] == port_cell[None, :]).astype(jnp.float32)
    source = port_hits[..., None] * excite[None]
    return (chosen + source).astype(jnp.bfloat16)


def shift(block, axis, step):
    count = lax.axis_size(axis)
    if step > 0:
        pairs = [(i, i + 1) for i in range(count - 1)]
    else:
        pairs = [(i + 1, i) for i in range(count - 1)]
    return lax.ppermute(block, axis, pairs)


def local(incoming, cell_type, bank, owner, port_cell, excite):
    cell_rows, cell_cols, port_count, order = incoming.shape
    col_count = lax.axis_size("col")
    row_count = lax.axis_size("row")
    row_at = lax.axis_index("row")
    col_at = lax.axis_index("col")
    width = cell_cols * col_count
    face = order // 4
    tagged = jnp.concatenate(
        [incoming, jnp.broadcast_to(cell_type.astype(incoming.dtype)[:, :, None, None], (cell_rows, cell_cols, port_count, 128))],
        axis=-1,
    )
    parts, tagged = broadcast_parts(bank[0, 0], owner, tagged)
    from_west, from_east = neighbours(tagged[:, 0], tagged[:, -1], "col")
    from_north, from_south = neighbours(tagged[0], tagged[-1], "row")
    row_ids = row_at * cell_rows + jnp.arange(cell_rows, dtype=jnp.int32)
    col_ids = col_at * cell_cols + jnp.arange(cell_cols, dtype=jnp.int32)
    flat_ids = (row_ids[:, None] * width + col_ids[None, :]).reshape(-1)
    ghost = jnp.concatenate([from_west, from_east, from_north, from_south], axis=0)
    ghost_ids = jnp.concatenate(
        [
            row_ids * width + col_at * cell_cols - 1,
            row_ids * width + (col_at + 1) * cell_cols,
            (row_at * cell_rows - 1) * width + col_ids,
            ((row_at + 1) * cell_rows) * width + col_ids,
        ]
    )
    cell_count = cell_rows * cell_cols
    all_traces = jnp.concatenate([incoming.reshape(cell_count, port_count, order), ghost[:, :, :order]], axis=0)
    all_kinds = jnp.concatenate([cell_type.reshape(-1), ghost[:, 0, order].astype(jnp.int32)])
    all_ids = jnp.concatenate([flat_ids, ghost_ids])
    first = sweep(all_traces, all_kinds, all_ids, parts, port_cell, excite)
    outgoing = first[:cell_count].reshape(cell_rows, cell_cols, port_count, order)
    ghost_out = first[cell_count:]
    zero = jnp.zeros_like(ghost_out[:cell_rows, :, :face])
    west_in = jnp.where(col_at > 0, ghost_out[:cell_rows, :, face : 2 * face], zero)
    east_in = jnp.where(col_at < col_count - 1, ghost_out[cell_rows : 2 * cell_rows, :, :face], zero)
    zero = jnp.zeros_like(ghost_out[:cell_cols, :, :face])
    at = 2 * cell_rows
    north_in = jnp.where(row_at > 0, ghost_out[at : at + cell_cols, :, 3 * face :], zero)
    south_in = jnp.where(
        row_at < row_count - 1, ghost_out[at + cell_cols : at + 2 * cell_cols, :, 2 * face : 3 * face], zero
    )
    traces = assemble(outgoing, west_in, east_in, north_in, south_in)
    kinds = cell_type.reshape(-1)
    for sweep_id in range(1, SWEEPS):
        outgoing = sweep(traces.reshape(cell_count, port_count, order), kinds, flat_ids, parts, port_cell, excite)
        outgoing = outgoing.reshape(cell_rows, cell_cols, port_count, order)
        if sweep_id + 1 < SWEEPS:
            traces = pass_traces(outgoing)
    return outgoing


def assemble(outgoing, west_in, east_in, north_in, south_in):
    face_len = outgoing.shape[-1] // 4
    west_face = outgoing[..., :face_len]
    east_face = outgoing[..., face_len : 2 * face_len]
    north_face = outgoing[..., 2 * face_len : 3 * face_len]
    south_face = outgoing[..., 3 * face_len :]
    new_west = jnp.concatenate([west_in[:, None], east_face[:, :-1]], axis=1)
    new_east = jnp.concatenate([west_face[:, 1:], east_in[:, None]], axis=1)
    new_north = jnp.concatenate([north_in[None], south_face[:-1]], axis=0)
    new_south = jnp.concatenate([north_face[1:], south_in[None]], axis=0)
    return jnp.concatenate([new_west, new_east, new_north, new_south], axis=-1)


def solution(mesh):
    in_specs = (
        P("row", "col", None, None),
        P("row", "col"),
        P("row", "col", None, None),
        P(),
        P(),
        P(),
    )
    out_specs = P("row", "col", None, None)
    return jax.shard_map(local, mesh=mesh, in_specs=in_specs, out_specs=out_specs, check_vma=False)
```

```python
import jax
import jax.numpy as jnp
from jax import lax
from jax.sharding import PartitionSpec as P

TYPES = 2
SWEEPS = 3


def neighbours(send_low, send_high, axis):
    count = lax.axis_size(axis)
    if count % 2:
        forward = [(i, i + 1) for i in range(count - 1)]
        backward = [(i + 1, i) for i in range(count - 1)]
        return lax.ppermute(send_high, axis, forward), lax.ppermute(send_low, axis, backward)
    even = lax.axis_index(axis) % 2 == 0
    inner = lax.ppermute(jnp.where(even, send_high, send_low), axis, [(i, i ^ 1) for i in range(count)])
    outer_pairs = [p for i in range(1, count - 1, 2) for p in ((i, i + 1), (i + 1, i))]
    outer = lax.ppermute(jnp.where(even, send_low, send_high), axis, outer_pairs)
    return jnp.where(even, outer, inner), jnp.where(even, inner, outer)


def pass_traces(outgoing):
    face_len = outgoing.shape[-1] // 4
    west_face = outgoing[..., :face_len]
    east_face = outgoing[..., face_len : 2 * face_len]
    north_face = outgoing[..., 2 * face_len : 3 * face_len]
    south_face = outgoing[..., 3 * face_len :]
    west_in, east_in = neighbours(west_face[:, 0], east_face[:, -1], "col")
    new_west = jnp.concatenate([west_in[:, None], east_face[:, :-1]], axis=1)
    new_east = jnp.concatenate([west_face[:, 1:], east_in[:, None]], axis=1)
    north_in, south_in = neighbours(north_face[0], south_face[-1], "row")
    new_north = jnp.concatenate([north_in[None], south_face[:-1]], axis=0)
    new_south = jnp.concatenate([north_face[1:], south_in[None]], axis=0)
    return jnp.concatenate([new_west, new_east, new_north, new_south], axis=-1)


def device_bits(axis):
    count = lax.axis_size(axis)
    bits = count.bit_length() - 1
    return bits if (1 << bits) == count else None


def swap(block, bits, core):
    count = lax.axis_size("col") * lax.axis_size("row")
    pairs = [(i, i ^ (1 << bits[(i >> core) & 1])) for i in range(count)]
    return lax.ppermute(block, ("row", "col"), pairs)


def scatter_gather(blocks, owner, orders, core, me, tie):
    stages = len(orders[0][0])
    full = (1 << stages) - 1
    my_core = (me >> core) & 1
    done_mask = [[0, 0] for _ in blocks]

    def pick(pair):
        return jnp.where(my_core == 1, pair[1], pair[0])

    for step in range(stages):
        gots, keeps = [], []
        for s, block in enumerate(blocks):
            bits = (orders[s][0][step], orders[s][1][step])
            mine = ((me >> pick(bits)) & 1) == 1
            if step == 0:
                half = block.shape[0] // 2
                keep = jnp.where(mine, block[half:], block[:half])
                keep = jnp.concatenate([keep] * TYPES, axis=1)
                give = jnp.where(mine, block[:half], block[half:])
            else:
                half = block.shape[0] // 2
                keep = jnp.where(mine, block[half:], block[:half])
                give = jnp.where(mine, block[:half], block[half:])
            got = swap(give, bits, core)
            keeps.append(keep)
            gots.append(jnp.concatenate([got] * TYPES, axis=1) if step == 0 else got)
        for s in range(len(blocks)):
            outside = pick([full & ~done_mask[s][0], full & ~done_mask[s][1]])
            have = ((me ^ owner) & outside) == 0
            lanes = jnp.repeat(have, keeps[s].shape[1] // TYPES)
            blocks[s] = jnp.where(lanes[None, :], keeps[s], gots[s])
            for c in range(2):
                done_mask[s][c] |= 1 << orders[s][c][step]
        blocks = list(lax.optimization_barrier(tuple(blocks)))
    blocks, tie = lax.optimization_barrier((tuple(blocks), tie))
    blocks = list(blocks)
    for step in reversed(range(stages)):
        gots = []
        for s, block in enumerate(blocks):
            gots.append(swap(block, (orders[s][0][step], orders[s][1][step]), core))
        for s in range(len(blocks)):
            mine = ((me >> pick((orders[s][0][step], orders[s][1][step]))) & 1) == 1
            blocks[s] = jnp.where(
                mine, jnp.concatenate([gots[s], blocks[s]], axis=0), jnp.concatenate([blocks[s], gots[s]], axis=0)
            )
        if step == stages - 1:
            blocks = list(lax.optimization_barrier(tuple(blocks)))
    return blocks, tie


def broadcast_parts(own_operator, owner, tie):
    col_bits = device_bits("col")
    row_bits = device_bits("row")
    me = lax.axis_index("row") * lax.axis_size("col") + lax.axis_index("col")
    stacked = jnp.stack([own_operator] * TYPES, axis=0)
    order_len = None if col_bits is None or row_bits is None else col_bits + row_bits
    if order_len is None or row_bits < 1 or col_bits < 1 or (own_operator.shape[0] >> order_len) < 8:
        mask = (me == owner)[:, None, None]
        summed = lax.psum(jnp.where(mask, stacked, jnp.zeros_like(stacked)), ("row", "col"))
        return [jnp.concatenate([summed[k] for k in range(TYPES)], axis=1)], tie
    core = col_bits
    middle = list(range(col_bits - 1)) + list(range(col_bits + 1, col_bits + row_bits))
    last = [col_bits - 1]
    streams = max(1, min(2, len(middle)))
    width = own_operator.shape[1]
    unit = width // 128
    sizes = [unit // streams + (1 if s < unit % streams else 0) for s in range(streams)]
    blocks, orders = [], []
    offset = 0
    for s in range(streams):
        cols = sizes[s] * 128
        pair = []
        for c in range(2):
            turn = (2 * s + c) % len(middle)
            pair.append([core] + middle[turn:] + middle[:turn] + last)
        orders.append(pair)
        blocks.append(own_operator[:, offset : offset + cols])
        offset += cols
    parts, tie = scatter_gather(blocks, owner, orders, core, me, tie)
    return parts, tie


def sweep(traces, kinds, ids, parts, port_cell, excite):
    count, port_count, order = traces.shape
    rows = traces.reshape(count * port_count, order)
    both = [jnp.dot(rows, part, preferred_element_type=jnp.float32) for part in parts]
    products = [
        jnp.concatenate(
            [prod[:, k * (prod.shape[1] // TYPES) : (k + 1) * (prod.shape[1] // TYPES)] for prod in both], axis=-1
        ).reshape(count, port_count, order)
        for k in range(TYPES)
    ]
    chosen = products[0]
    for k in range(1, TYPES):
        chosen = jnp.where((kinds == k)[:, None, None], products[k], chosen)
    port_hits = (ids[:, None] == port_cell[None, :]).astype(jnp.float32)
    source = port_hits[..., None] * excite[None]
    return (chosen + source).astype(jnp.bfloat16)


def shift(block, axis, step):
    count = lax.axis_size(axis)
    if step > 0:
        pairs = [(i, i + 1) for i in range(count - 1)]
    else:
        pairs = [(i + 1, i) for i in range(count - 1)]
    return lax.ppermute(block, axis, pairs)


def local(incoming, cell_type, bank, owner, port_cell, excite):
    cell_rows, cell_cols, port_count, order = incoming.shape
    col_count = lax.axis_size("col")
    row_count = lax.axis_size("row")
    row_at = lax.axis_index("row")
    col_at = lax.axis_index("col")
    width = cell_cols * col_count
    face = order // 4
    tagged = jnp.concatenate(
        [incoming, jnp.broadcast_to(cell_type.astype(incoming.dtype)[:, :, None, None], (cell_rows, cell_cols, port_count, 128))],
        axis=-1,
    )
    parts, tagged = broadcast_parts(bank[0, 0], owner, tagged)
    from_west, from_east = neighbours(tagged[:, 0], tagged[:, -1], "col")
    from_north, from_south = neighbours(tagged[0], tagged[-1], "row")
    row_ids = row_at * cell_rows + jnp.arange(cell_rows, dtype=jnp.int32)
    col_ids = col_at * cell_cols + jnp.arange(cell_cols, dtype=jnp.int32)
    flat_ids = (row_ids[:, None] * width + col_ids[None, :]).reshape(-1)
    ghost = jnp.concatenate([from_west, from_east, from_north, from_south], axis=0)
    ghost_ids = jnp.concatenate(
        [
            row_ids * width + col_at * cell_cols - 1,
            row_ids * width + (col_at + 1) * cell_cols,
            (row_at * cell_rows - 1) * width + col_ids,
            ((row_at + 1) * cell_rows) * width + col_ids,
        ]
    )
    cell_count = cell_rows * cell_cols
    all_traces = jnp.concatenate([incoming.reshape(cell_count, port_count, order), ghost[:, :, :order]], axis=0)
    all_kinds = jnp.concatenate([cell_type.reshape(-1), ghost[:, 0, order].astype(jnp.int32)])
    all_ids = jnp.concatenate([flat_ids, ghost_ids])
    first = sweep(all_traces, all_kinds, all_ids, parts, port_cell, excite)
    outgoing = first[:cell_count].reshape(cell_rows, cell_cols, port_count, order)
    ghost_out = first[cell_count:]
    zero = jnp.zeros_like(ghost_out[:cell_rows, :, :face])
    west_in = jnp.where(col_at > 0, ghost_out[:cell_rows, :, face : 2 * face], zero)
    east_in = jnp.where(col_at < col_count - 1, ghost_out[cell_rows : 2 * cell_rows, :, :face], zero)
    zero = jnp.zeros_like(ghost_out[:cell_cols, :, :face])
    at = 2 * cell_rows
    north_in = jnp.where(row_at > 0, ghost_out[at : at + cell_cols, :, 3 * face :], zero)
    south_in = jnp.where(
        row_at < row_count - 1, ghost_out[at + cell_cols : at + 2 * cell_cols, :, 2 * face : 3 * face], zero
    )
    traces = assemble(outgoing, west_in, east_in, north_in, south_in)
    kinds = cell_type.reshape(-1)
    for sweep_id in range(1, SWEEPS):
        outgoing = sweep(traces.reshape(cell_count, port_count, order), kinds, flat_ids, parts, port_cell, excite)
        outgoing = outgoing.reshape(cell_rows, cell_cols, port_count, order)
        if sweep_id + 1 < SWEEPS:
            traces = pass_traces(outgoing)
    return outgoing


def assemble(outgoing, west_in, east_in, north_in, south_in):
    face_len = outgoing.shape[-1] // 4
    west_face = outgoing[..., :face_len]
    east_face = outgoing[..., face_len : 2 * face_len]
    north_face = outgoing[..., 2 * face_len : 3 * face_len]
    south_face = outgoing[..., 3 * face_len :]
    new_west = jnp.concatenate([west_in[:, None], east_face[:, :-1]], axis=1)
    new_east = jnp.concatenate([west_face[:, 1:], east_in[:, None]], axis=1)
    new_north = jnp.concatenate([north_in[None], south_face[:-1]], axis=0)
    new_south = jnp.concatenate([north_face[1:], south_in[None]], axis=0)
    return jnp.concatenate([new_west, new_east, new_north, new_south], axis=-1)


def solution(mesh):
    in_specs = (
        P("row", "col", None, None),
        P("row", "col"),
        P("row", "col", None, None),
        P(),
        P(),
        P(),
    )
    out_specs = P("row", "col", None, None)
    return jax.shard_map(local, mesh=mesh, in_specs=in_specs, out_specs=out_specs, check_vma=False)
```
